32 devices in a mesh: section: 4 (over x, core), expert: 8 (over z, y).
Axes of the slice: x: 2, y: 2, z: 4, core: 2. Of those that a mesh axis runs over, the one named last changes fastest.
Arguments:
- layer_inputs: bfloat16 [4, 8, 128, 2048], P('section', None, 'expert'), may hold values from -6 to 6
- top_grad: bfloat16 [8, 128, 2048], P('section', 'expert'), may hold values from -6 to 6
- expert_ids: int32 [4, 8, 128, 4], P('section', None, 'expert'), may hold values from 0 to 7, all different within a row; in each aligned block of 16 rows (0 to 15, 16 to 31, ..., all dimensions but the last counted through in order) at most 9 rows name the same one
- router: bfloat16 [4, 2048, 8], P('section'), may hold values from -0.125 to 0.125
- norm_gain: bfloat16 [4, 2048], P('section'), may hold values from 0.099609375 to 1.8984375
- w_gate: bfloat16 [4, 8, 2048, 1024], P('section', 'expert'), may hold values from -0.125 to 0.125
- w_up: bfloat16 [4, 8, 2048, 1024], P('section', 'expert'), may hold values from -0.125 to 0.125
- w_down: bfloat16 [4, 8, 1024, 2048], P('section', 'expert'), may hold values from -0.1875 to 0.1875
Outputs:
- input_grads: bfloat16 [4, 8, 128, 2048], P('section', None, 'expert')
The draws below stay inside these ranges and needn't reach their ends.
Inputs may be any that keep to these rules, and one draw needn't show every extreme that they name: `expert_ids`: each token names 4 different experts. Among the 16 tokens of one device in one micro-batch of one layer, no expert is named by more than 9 of them, and in some of these blocks one expert is named by exactly 9.
All inputs are finite; a program needn't handle non-finite values.
Results may differ from the reference program's by a relative error of at most 0.015.
Values may be sent and summed in bfloat16 or wider, within the bound.
No kernel may reach another device: no remote copies, remote signals or barrier semaphores. Data moves between devices by JAX's collectives and lax.ppermute only.
A program may use at most 128 MiB of HBM per device.

```python
import math
import jax
import jax.numpy as jnp
import numpy as np
from jax import lax

D = 2048
FF = 1024
MICRO = 8
TOK_DEV = 16
LAYERS = 4
EXPERTS = 8
TOPK = 4
TOKENS = 128
MOST = 9
N_EXPERT = 8


def steps_of(stream_key, extent, cuts, smallest, top_value):
    level, own = 1.0, jax.random.fold_in(stream_key, 6)
    for axis_at, shards_of in cuts:
        heights = jnp.exp(jax.random.uniform(jax.random.fold_in(own, axis_at), (shards_of,), jnp.float32, smallest / len(cuts), top_value / len(cuts)))
        level = level * jnp.repeat(heights, extent[axis_at] // shards_of).reshape([-1 if axis == axis_at else 1 for axis in range(len(extent))])
    return level


def deal_out(stream_key, own, number, rows, amount, top, reach, skew):
    sequence = jax.random.permutation(stream_key, amount)
    crowded, ordinary = load_shares(amount, rows * top, reach, skew, True), load_shares(amount, rows * top, reach, skew, False)
    places = jnp.arange(amount)

    def named(sizes, rotation):
        used = int((sizes > 0).sum())
        fixed = max(1, used // 4)
        passed = fixed + (places - fixed + rotation * (used - fixed)) % max(1, amount - fixed)
        return jnp.zeros((amount,), jnp.int32).at[sequence[jnp.where(places < fixed, places, passed)]].set(jnp.asarray(sizes, jnp.int32))

    sizes = jnp.where(number % 4 == 0, named(crowded, number // 4), named(ordinary, number - number // 4 - 1))
    mixed = jax.random.permutation(jax.random.fold_in(own, 3), amount)
    giver, sink = mixed[0:amount // 2 * 2:2], mixed[1:amount // 2 * 2:2]
    slack = jnp.minimum(sizes[giver] - 1, reach - sizes[sink]) // 2
    slack = jnp.where((giver == sequence[0]) | (sink == sequence[0]) | (sizes[sink] == 0), 0, jnp.maximum(slack, 0))
    passed = jax.random.randint(jax.random.fold_in(own, 4), (amount // 2,), 0, 1 << 20) % (slack + 1)
    sizes = sizes.at[giver].add(-passed).at[sink].add(passed)
    members = jnp.searchsorted(jnp.cumsum(sizes), jnp.arange(rows * top), side="right").astype(jnp.int32)
    listing = members.reshape(top, rows).T
    listing = listing[jax.random.permutation(jax.random.fold_in(own, 1), rows)]
    rotation = jax.random.randint(jax.random.fold_in(own, 2), (rows, 1), 0, top)
    return jnp.take_along_axis(listing, (jnp.arange(top)[None, :] + rotation) % top, axis=1)


def load_shares(amount, total, most, skew, full):
    portions = [(1 << 20) // math.isqrt(grade ** skew) + 1 for grade in range(1, amount + 1)]
    largest = most if full else min(most, max(-(-total // amount), total * portions[0] // sum(portions)))
    least = 1 if total - largest >= amount - 1 else 0
    counts, spare = [largest] + [least] * (amount - 1), total - largest - least * (amount - 1)
    while spare > 0:
        free = [i for i in range(1, amount) if counts[i] < largest] or [i for i in range(1, amount) if counts[i] < most]
        mass, left = sum([portions[i] for i in free]), spare
        for i in free:
            more = min(most - counts[i], max(1, left * portions[i] // mass), spare)
            counts[i] = counts[i] + more
            spare = spare - more
    return np.array(counts)


def centred(own_key, dims, deviation, most, shards=(), held_as=jnp.bfloat16):
    entries = jax.random.normal(own_key, dims, jnp.float32) * deviation
    if len(shards) > 0:
        entries = steps_of(own_key, dims, shards, -0.22, 0.18) * entries
    return jnp.clip(entries, min=-most, max=most).astype(held_as)


def setup_inputs(seed: int = 0) -> dict:
    key_list = jax.random.split(jax.random.key(seed), 9)
    layer_inputs = centred(key_list[0], (LAYERS, MICRO, TOKENS, D), 1.0, 6.0, ((0, 4), (2, 8)))
    top_grad = centred(key_list[1], (MICRO, TOKENS, D), 1.0, 6.0, ((0, 4), (1, 8)))
    expert_ids_keys = jax.random.split(jax.random.fold_in(key_list[2], 1), LAYERS * MICRO * TOKENS // TOK_DEV)
    expert_ids_turns = jax.random.permutation(jax.random.fold_in(key_list[2], 3), LAYERS * MICRO * TOKENS // TOK_DEV)
    expert_ids = jax.vmap(lambda own, number: deal_out(jax.random.fold_in(key_list[2], 2), own, number, TOK_DEV, N_EXPERT, TOPK, MOST, 2))(expert_ids_keys, expert_ids_turns).reshape((LAYERS, MICRO, TOKENS, TOPK))
    router = centred(key_list[3], (LAYERS, D, EXPERTS), D ** -0.5, 0.125, ((0, 4),))
    norm_gain = jnp.clip(1.0 + 0.18 * jax.random.normal(key_list[4], (LAYERS, D), jnp.float32), 0.099609375, 1.8984375).astype(jnp.bfloat16)
    w_gate = centred(key_list[5], (LAYERS, EXPERTS, D, FF), D ** -0.5, 0.125, ((0, 4), (1, 8)))
    w_up = centred(key_list[6], (LAYERS, EXPERTS, D, FF), D ** -0.5, 0.125, ((0, 4), (1, 8)))
    w_down = centred(key_list[7], (LAYERS, EXPERTS, FF, D), FF ** -0.5, 0.1875, ((0, 4), (1, 8)))
    return dict(layer_inputs=layer_inputs, top_grad=top_grad, expert_ids=expert_ids, router=router, norm_gain=norm_gain, w_gate=w_gate, w_up=w_up, w_down=w_down)


def prepare(x_rows, gain):
    x_float = x_rows.astype(jnp.float32)
    inverse = lax.rsqrt(lax.optimization_barrier(jnp.mean(x_float * x_float, axis=-1, keepdims=True)) + 1e-05)
    normed = (x_float * inverse * gain).astype(jnp.bfloat16)
    return (x_float, inverse, normed)

def expert_rows(normed_rows, grad_rows, gate_w, up_w, down_w):
    gate = jnp.dot(normed_rows, gate_w, preferred_element_type=jnp.float32)
    up_rows = jnp.dot(normed_rows, up_w, preferred_element_type=jnp.float32)
    squash = jax.nn.sigmoid(gate)
    active = gate * squash
    hidden = (active * up_rows).astype(jnp.bfloat16)
    output = jnp.dot(hidden, down_w, preferred_element_type=jnp.float32)
    dprob = lax.optimization_barrier(jnp.sum(output * grad_rows.astype(jnp.float32), axis=-1))
    dhidden = lax.dot_general(grad_rows, down_w, (((1,), (1,)), ((), ())), preferred_element_type=jnp.float32)
    dgate = (dhidden * up_rows * squash * (1.0 + gate * (1.0 - squash))).astype(jnp.bfloat16)
    dup = (dhidden * active).astype(jnp.bfloat16)
    returned = lax.dot_general(dgate, gate_w, (((1,), (1,)), ((), ())), preferred_element_type=jnp.float32)
    returned = returned + lax.dot_general(dup, up_w, (((1,), (1,)), ((), ())), preferred_element_type=jnp.float32)
    return (returned.astype(jnp.bfloat16), dprob)

def finish(x_float, inverse, normed, gain, router_layer, ids, grad_in, pair_back, pair_prob):
    logits = jnp.dot(normed, router_layer, preferred_element_type=jnp.float32)
    raised = jnp.exp(logits)
    probs = raised / lax.optimization_barrier(jnp.sum(raised, axis=-1, keepdims=True))
    choose = (ids[..., None] == jnp.arange(router_layer.shape[1], dtype=jnp.int32)).astype(jnp.float32)
    picked = lax.optimization_barrier(jnp.sum(probs[..., None, :] * choose, axis=-1))
    dfull = lax.optimization_barrier(jnp.sum(pair_prob[..., None] * choose, axis=-2))
    dlogit = probs * (dfull - lax.optimization_barrier(jnp.sum(probs * dfull, axis=-1, keepdims=True)))
    router_term = jnp.dot(dlogit, router_layer.astype(jnp.float32).T, precision=lax.Precision.HIGHEST)
    dnormed = lax.optimization_barrier(jnp.sum(picked[..., None] * pair_back, axis=-2)) + router_term
    scaled = gain * dnormed
    inner = lax.optimization_barrier(jnp.mean(x_float * scaled, axis=-1, keepdims=True))
    result = grad_in.astype(jnp.float32) + inverse * scaled - x_float * inverse * inverse * inverse * inner
    return result.astype(jnp.bfloat16)

def reference(layer_inputs, top_grad, expert_ids, router, norm_gain, w_gate, w_up, w_down):
    pairs = TOPK * TOK_DEV
    total = N_EXPERT * MICRO * N_EXPERT * MOST
    micro_index = jnp.arange(MICRO, dtype=jnp.int32)[:, None, None]
    block_index = jnp.arange(N_EXPERT, dtype=jnp.int32)[None, :, None]
    grad_in = top_grad
    collected = []
    for layer in reversed(range(LAYERS)):
        gain = norm_gain[layer].astype(jnp.float32)
        x_float, inverse, normed = prepare(layer_inputs[layer], gain)
        ids = expert_ids[layer]
        block_ids = ids.reshape(MICRO, N_EXPERT, pairs)
        onehot = (block_ids[..., None] == jnp.arange(N_EXPERT, dtype=jnp.int32)).astype(jnp.int32)
        ranks = lax.optimization_barrier(jnp.sum(onehot * (jnp.cumsum(onehot, axis=2) - 1), axis=-1))
        where = (((block_ids * MICRO + micro_index) * N_EXPERT + block_index) * MOST + ranks).reshape(-1)
        normed_pairs = jnp.repeat(normed, TOPK, axis=1).reshape(-1, D)
        grad_pairs = jnp.repeat(grad_in, TOPK, axis=1).reshape(-1, D)
        normed_buf = jnp.zeros((total, D), jnp.bfloat16).at[where].set(normed_pairs)
        grad_buf = jnp.zeros((total, D), jnp.bfloat16).at[where].set(grad_pairs)
        normed_buf = normed_buf.reshape(N_EXPERT, -1, D)
        grad_buf = grad_buf.reshape(N_EXPERT, -1, D)

        def one_expert(operands):
            return expert_rows(operands[0], operands[1], operands[2], operands[3], operands[4])
        returned, dprob = lax.map(one_expert, (normed_buf, grad_buf, w_gate[layer], w_up[layer], w_down[layer]))
        pair_back = returned.reshape(total, D)[where].astype(jnp.float32).reshape(MICRO, TOKENS, TOPK, D)
        pair_prob = dprob.reshape(total)[where].reshape(MICRO, TOKENS, TOPK)
        result = finish(x_float, inverse, normed, gain, router[layer], ids, grad_in, pair_back, pair_prob)
        collected.append(result)
        grad_in = result
    return jnp.stack(collected[::-1])
```

```python
import jax
import jax.numpy as jnp
from jax import lax
from jax.sharding import PartitionSpec as P

CHUNK = 2


def shifted(shard, axis, by):
    devices = lax.axis_size(axis)
    pairs = [(i, i + by) for i in range(devices) if 0 <= i + by < devices]
    return lax.ppermute(shard, axis, pairs)


def prepare(x_rows, gain):
    x_float = x_rows.astype(jnp.float32)
    inverse = lax.rsqrt(jnp.mean(x_float * x_float, axis=-1, keepdims=True) + 1e-05)
    normed = (x_float * inverse * gain).astype(jnp.bfloat16)
    return (x_float, inverse, normed)


def selection(ids, experts, capacity):
    pair_ids = ids.reshape(-1)
    onehot = (pair_ids[:, None] == jnp.arange(experts, dtype=jnp.int32)[None, :]).astype(jnp.int32)
    ranks = jnp.sum(onehot * (jnp.cumsum(onehot, axis=0) - 1), axis=1)
    target = pair_ids * capacity + ranks
    return (target[:, None] == jnp.arange(experts * capacity, dtype=jnp.int32)[None, :]).astype(
        jnp.bfloat16
    )


def pack_rows(select, rows, per_token):
    repeated = jnp.repeat(rows, per_token, axis=1)
    packed = jnp.einsum("mps,mpw->msw", select, repeated, preferred_element_type=jnp.float32)
    return packed.astype(jnp.bfloat16)


def finish(x_float, inverse, gain, router_layer, probs, choose, picked, grad_in, pair_back, pair_prob):
    dfull = jnp.sum(pair_prob[..., None] * choose, axis=-2)
    dlogit = probs * (dfull - jnp.sum(probs * dfull, axis=-1, keepdims=True))
    router_term = jnp.dot(
        dlogit, router_layer.astype(jnp.float32).T, precision=lax.Precision.HIGHEST
    )
    dnormed = jnp.sum(picked[..., None] * pair_back, axis=-2) + router_term
    scaled = gain * dnormed
    inner = jnp.mean(x_float * scaled, axis=-1, keepdims=True)
    result = (
        grad_in.astype(jnp.float32)
        + inverse * scaled
        - x_float * inverse * inverse * inverse * inner
    )
    return result.astype(jnp.bfloat16)


def shards(layer_inputs, top_grad, expert_ids, router, norm_gain, w_gate, w_up, w_down):
    segments = lax.axis_size("section")
    experts = lax.axis_size("expert")
    segment_index = lax.axis_index("section")
    micro = layer_inputs.shape[1]
    tok_rows = layer_inputs.shape[2]
    width = layer_inputs.shape[3]
    per_token = expert_ids.shape[3]
    capacity = min(tok_rows, per_token * tok_rows // experts + max(1, tok_rows // 16))
    slots = experts * capacity
    chunk = CHUNK if micro % CHUNK == 0 else 1
    chunks = micro // chunk
    lanes = 128
    gain = norm_gain[0].astype(jnp.float32)
    router_layer = router[0]
    gate_w = w_gate[0, 0]
    up_w = w_up[0, 0]
    down_w = w_down[0, 0]
    ids = expert_ids[0]
    x_float, inverse, normed = prepare(layer_inputs[0], gain)
    top_full = lax.all_gather(top_grad, "section", axis=0, tiled=True)

    select = jax.vmap(lambda i: selection(i, experts, capacity))(ids)
    sent_normed = pack_rows(select, normed, per_token).reshape(micro, experts, capacity, width)
    got_normed = lax.all_to_all(sent_normed, "expert", split_axis=1, concat_axis=1, tiled=True)
    rows = got_normed.reshape(micro * slots, width)
    gate = jnp.dot(rows, gate_w, preferred_element_type=jnp.float32)
    up_rows = jnp.dot(rows, up_w, preferred_element_type=jnp.float32)
    squash = jax.nn.sigmoid(gate)
    active = gate * squash
    hidden = (active * up_rows).astype(jnp.bfloat16)
    output = jnp.dot(hidden, down_w, preferred_element_type=jnp.float32)
    factor = up_rows * squash * (1.0 + gate * (1.0 - squash))
    output = output.reshape(micro, slots, width)
    factor = factor.reshape(micro, slots, -1)
    active = active.reshape(micro, slots, -1)

    logits = jnp.dot(normed, router_layer, preferred_element_type=jnp.float32)
    raised = jnp.exp(logits)
    probs = raised / jnp.sum(raised, axis=-1, keepdims=True)
    choose = (ids[..., None] == jnp.arange(router_layer.shape[1], dtype=jnp.int32)).astype(
        jnp.float32
    )
    picked = jnp.sum(probs[..., None, :] * choose, axis=-1)

    def take(values, start):
        return lax.dynamic_slice_in_dim(values, start, chunk, 0)

    def advance(step, carry):
        previous, collected = carry
        arrived = shifted(previous, "section", -1)
        position = step - (segments - 1 - segment_index)
        working = jnp.logical_and(position >= 0, position < chunks)
        start = jnp.clip(position, 0, chunks - 1) * chunk
        grad_in = jnp.where(segment_index == segments - 1, take(top_full, start), arrived)
        select_now = take(select, start)
        sent_grad = pack_rows(select_now, grad_in, per_token).reshape(
            chunk, experts, capacity, width
        )
        got_grad = lax.all_to_all(sent_grad, "expert", split_axis=1, concat_axis=1, tiled=True)
        rows_grad = got_grad.reshape(chunk * slots, width)
        out_now = take(output, start).reshape(chunk * slots, width)
        dprob = jnp.sum(out_now * rows_grad.astype(jnp.float32), axis=-1)
        dhidden = lax.dot_general(
            rows_grad, down_w, (((1,), (1,)), ((), ())), preferred_element_type=jnp.float32
        )
        factor_now = take(factor, start).reshape(chunk * slots, -1)
        active_now = take(active, start).reshape(chunk * slots, -1)
        dgate = (dhidden * factor_now).astype(jnp.bfloat16)
        dup = (dhidden * active_now).astype(jnp.bfloat16)
        returned = lax.dot_general(
            dgate, gate_w, (((1,), (1,)), ((), ())), preferred_element_type=jnp.float32
        )
        returned = returned + lax.dot_general(
            dup, up_w, (((1,), (1,)), ((), ())), preferred_element_type=jnp.float32
        )
        high = dprob.astype(jnp.bfloat16)
        low = (dprob - high.astype(jnp.float32)).astype(jnp.bfloat16)
        column = lax.broadcasted_iota(jnp.int32, (chunk * slots, lanes), 1)
        extra = jnp.where(column == 0, high[:, None], jnp.where(column == 1, low[:, None], 0))
        packed = jnp.concatenate([returned.astype(jnp.bfloat16), extra.astype(jnp.bfloat16)], axis=1)
        packed = packed.reshape(chunk, experts, capacity, width + lanes)
        back = lax.all_to_all(packed, "expert", split_axis=1, concat_axis=1, tiled=True)
        back = back.reshape(chunk, slots, width + lanes)
        pair = jnp.einsum("mps,msw->mpw", select_now, back, preferred_element_type=jnp.float32)
        pair_back = pair[..., :width].reshape(chunk, tok_rows, per_token, width)
        pair_prob = (pair[..., width] + pair[..., width + 1]).reshape(chunk, tok_rows, per_token)
        result = finish(
            take(x_float, start),
            take(inverse, start),
            gain,
            router_layer,
            take(probs, start),
            take(choose, start),
            take(picked, start),
            grad_in,
            pair_back,
            pair_prob,
        )
        retained = take(collected, start)
        collected = lax.dynamic_update_slice_in_dim(
            collected, jnp.where(working, result, retained), start, 0
        )
        return (result, collected)

    begin = (
        jnp.zeros((chunk, tok_rows, width), jnp.bfloat16),
        jnp.zeros((micro, tok_rows, width), jnp.bfloat16),
    )
    final_grad, collected = lax.fori_loop(0, chunks + segments - 1, advance, begin)
    return collected.reshape(1, micro, tok_rows, width)


def solution(mesh):
    placed = (
        P("section", None, "expert", None),
        P("section", "expert", None),
        P("section", None, "expert", None),
        P("section", None, None),
        P("section", None),
        P("section", "expert", None, None),
        P("section", "expert", None, None),
        P("section", "expert", None, None),
    )
    return jax.shard_map(
        shards,
        mesh=mesh,
        in_specs=placed,
        out_specs=P("section", None, "expert", None),
        check_vma=False,
    )
```

```python
import jax
import jax.numpy as jnp
from jax import lax
from jax.sharding import PartitionSpec as P

CHUNK = 2


def shifted(shard, axis, by):
    devices = lax.axis_size(axis)
    pairs = [(i, i + by) for i in range(devices) if 0 <= i + by < devices]
    return lax.ppermute(shard, axis, pairs)


def prepare(x_rows, gain):
    x_float = x_rows.astype(jnp.float32)
    inverse = lax.rsqrt(jnp.mean(x_float * x_float, axis=-1, keepdims=True) + 1e-05)
    normed = (x_float * inverse * gain).astype(jnp.bfloat16)
    return (x_float, inverse, normed)


def selection(ids, experts, capacity):
    pair_ids = ids.reshape(-1)
    onehot = (pair_ids[:, None] == jnp.arange(experts, dtype=jnp.int32)[None, :]).astype(jnp.int32)
    ranks = jnp.sum(onehot * (jnp.cumsum(onehot, axis=0) - 1), axis=1)
    target = pair_ids * capacity + ranks
    return (target[:, None] == jnp.arange(experts * capacity, dtype=jnp.int32)[None, :]).astype(
        jnp.bfloat16
    )


def pack_rows(select, rows, per_token):
    repeated = jnp.repeat(rows, per_token, axis=1)
    packed = jnp.einsum("mps,mpw->msw", select, repeated, preferred_element_type=jnp.float32)
    return packed.astype(jnp.bfloat16)


def finish(x_float, inverse, gain, router_layer, probs, choose, picked, grad_in, pair_back, pair_prob):
    dfull = jnp.sum(pair_prob[..., None] * choose, axis=-2)
    dlogit = probs * (dfull - jnp.sum(probs * dfull, axis=-1, keepdims=True))
    router_term = jnp.dot(
        dlogit, router_layer.astype(jnp.float32).T, precision=lax.Precision.HIGHEST
    )
    dnormed = jnp.sum(picked[..., None] * pair_back, axis=-2) + router_term
    scaled = gain * dnormed
    inner = jnp.mean(x_float * scaled, axis=-1, keepdims=True)
    result = (
        grad_in.astype(jnp.float32)
        + inverse * scaled
        - x_float * inverse * inverse * inverse * inner
    )
    return result.astype(jnp.bfloat16)


def shards(layer_inputs, top_grad, expert_ids, router, norm_gain, w_gate, w_up, w_down):
    segments = lax.axis_size("section")
    experts = lax.axis_size("expert")
    segment_index = lax.axis_index("section")
    micro = layer_inputs.shape[1]
    tok_rows = layer_inputs.shape[2]
    width = layer_inputs.shape[3]
    per_token = expert_ids.shape[3]
    capacity = min(tok_rows, per_token * tok_rows // experts + max(1, tok_rows // 16))
    slots = experts * capacity
    chunk = CHUNK if micro % CHUNK == 0 else 1
    chunks = micro // chunk
    lanes = 128
    gain = norm_gain[0].astype(jnp.float32)
    router_layer = router[0]
    gate_w = w_gate[0, 0]
    up_w = w_up[0, 0]
    down_w = w_down[0, 0]
    ids = expert_ids[0]
    x_float, inverse, normed = prepare(layer_inputs[0], gain)
    top_full = lax.all_gather(top_grad, "section", axis=0, tiled=True)

    select = jax.vmap(lambda i: selection(i, experts, capacity))(ids)
    sent_normed = pack_rows(select, normed, per_token).reshape(micro, experts, capacity, width)
    got_normed = lax.all_to_all(sent_normed, "expert", split_axis=1, concat_axis=1, tiled=True)
    rows = got_normed.reshape(micro * slots, width)
    gate = jnp.dot(rows, gate_w, preferred_element_type=jnp.float32)
    up_rows = jnp.dot(rows, up_w, preferred_element_type=jnp.float32)
    squash = jax.nn.sigmoid(gate)
    active = gate * squash
    hidden = (active * up_rows).astype(jnp.bfloat16)
    factor = up_rows * squash * (1.0 + gate * (1.0 - squash))
    hidden = hidden.reshape(micro, slots, -1)
    factor = factor.reshape(micro, slots, -1)
    active = active.reshape(micro, slots, -1)

    logits = jnp.dot(normed, router_layer, preferred_element_type=jnp.float32)
    raised = jnp.exp(logits)
    probs = raised / jnp.sum(raised, axis=-1, keepdims=True)
    choose = (ids[..., None] == jnp.arange(router_layer.shape[1], dtype=jnp.int32)).astype(
        jnp.float32
    )
    picked = jnp.sum(probs[..., None, :] * choose, axis=-1)

    def take(values, start):
        return lax.dynamic_slice_in_dim(values, start, chunk, 0)

    def advance(step, carry):
        previous, collected = carry
        arrived = shifted(previous, "section", -1)
        position = step - (segments - 1 - segment_index)
        working = jnp.logical_and(position >= 0, position < chunks)
        start = jnp.clip(position, 0, chunks - 1) * chunk
        grad_in = jnp.where(segment_index == segments - 1, take(top_full, start), arrived)
        select_now = take(select, start)
        sent_grad = pack_rows(select_now, grad_in, per_token).reshape(
            chunk, experts, capacity, width
        )
        got_grad = lax.all_to_all(sent_grad, "expert", split_axis=1, concat_axis=1, tiled=True)
        rows_grad = got_grad.reshape(chunk * slots, width)
        dhidden = lax.dot_general(
            rows_grad, down_w, (((1,), (1,)), ((), ())), preferred_element_type=jnp.float32
        )
        hidden_now = take(hidden, start).reshape(chunk * slots, -1)
        dprob = jnp.sum(hidden_now.astype(jnp.float32) * dhidden, axis=-1)
        factor_now = take(factor, start).reshape(chunk * slots, -1)
        active_now = take(active, start).reshape(chunk * slots, -1)
        dgate = (dhidden * factor_now).astype(jnp.bfloat16)
        dup = (dhidden * active_now).astype(jnp.bfloat16)
        returned = lax.dot_general(
            dgate, gate_w, (((1,), (1,)), ((), ())), preferred_element_type=jnp.float32
        )
        returned = returned + lax.dot_general(
            dup, up_w, (((1,), (1,)), ((), ())), preferred_element_type=jnp.float32
        )
        high = dprob.astype(jnp.bfloat16)
        low = (dprob - high.astype(jnp.float32)).astype(jnp.bfloat16)
        column = lax.broadcasted_iota(jnp.int32, (chunk * slots, lanes), 1)
        extra = jnp.where(column == 0, high[:, None], jnp.where(column == 1, low[:, None], 0))
        packed = jnp.concatenate([returned.astype(jnp.bfloat16), extra.astype(jnp.bfloat16)], axis=1)
        packed = packed.reshape(chunk, experts, capacity, width + lanes)
        back = lax.all_to_all(packed, "expert", split_axis=1, concat_axis=1, tiled=True)
        back = back.reshape(chunk, slots, width + lanes)
        pair = jnp.einsum("mps,msw->mpw", select_now, back, preferred_element_type=jnp.float32)
        pair_back = pair[..., :width].reshape(chunk, tok_rows, per_token, width)
        pair_prob = (pair[..., width] + pair[..., width + 1]).reshape(chunk, tok_rows, per_token)
        result = finish(
            take(x_float, start),
            take(inverse, start),
            gain,
            router_layer,
            take(probs, start),
            take(choose, start),
            take(picked, start),
            grad_in,
            pair_back,
            pair_prob,
        )
        retained = take(collected, start)
        collected = lax.dynamic_update_slice_in_dim(
            collected, jnp.where(working, result, retained), start, 0
        )
        return (result, collected)

    begin = (
        jnp.zeros((chunk, tok_rows, width), jnp.bfloat16),
        jnp.zeros((micro, tok_rows, width), jnp.bfloat16),
    )
    final_grad, collected = lax.fori_loop(0, chunks + segments - 1, advance, begin)
    return collected.reshape(1, micro, tok_rows, width)


def solution(mesh):
    placed = (
        P("section", None, "expert", None),
        P("section", "expert", None),
        P("section", None, "expert", None),
        P("section", None, None),
        P("section", None),
        P("section", "expert", None, None),
        P("section", "expert", None, None),
        P("section", "expert", None, None),
    )
    return jax.shard_map(
        shards,
        mesh=mesh,
        in_specs=placed,
        out_specs=P("section", None, "expert", None),
        check_vma=False,
    )
```

```python
import jax
import jax.numpy as jnp
from jax import lax
from jax.sharding import PartitionSpec as P

CHUNK = 2


def shifted(shard, axis, by):
    devices = lax.axis_size(axis)
    pairs = [(i, i + by) for i in range(devices) if 0 <= i + by < devices]
    return lax.ppermute(shard, axis, pairs)


def exchange(values):
    shape = values.shape
    folded = values.reshape(shape[:-1] + (shape[-1] // 128, 128))
    folded = lax.all_to_all(folded, "expert", split_axis=1, concat_axis=1, tiled=True)
    return folded.reshape(shape)


def prepare(x_rows, gain):
    x_float = x_rows.astype(jnp.float32)
    inverse = lax.rsqrt(jnp.mean(x_float * x_float, axis=-1, keepdims=True) + 1e-05)
    normed = (x_float * inverse * gain).astype(jnp.bfloat16)
    return (x_float, inverse, normed)


def selection(ids, experts, capacity):
    pair_ids = ids.reshape(-1)
    onehot = (pair_ids[:, None] == jnp.arange(experts, dtype=jnp.int32)[None, :]).astype(jnp.int32)
    ranks = jnp.sum(onehot * (jnp.cumsum(onehot, axis=0) - 1), axis=1)
    target = pair_ids * capacity + ranks
    return (target[:, None] == jnp.arange(experts * capacity, dtype=jnp.int32)[None, :]).astype(
        jnp.bfloat16
    )


def pack_rows(select, rows, per_token):
    repeated = jnp.repeat(rows, per_token, axis=1)
    packed = jnp.einsum("mps,mpw->msw", select, repeated, preferred_element_type=jnp.float32)
    return packed.astype(jnp.bfloat16)


def finish(x_float, inverse, gain, router_layer, probs, choose, picked, grad_in, pair_back, pair_prob):
    dfull = jnp.sum(pair_prob[..., None] * choose, axis=-2)
    dlogit = probs * (dfull - jnp.sum(probs * dfull, axis=-1, keepdims=True))
    router_term = jnp.dot(
        dlogit, router_layer.astype(jnp.float32).T, precision=lax.Precision.HIGHEST
    )
    dnormed = jnp.sum(picked[..., None] * pair_back, axis=-2) + router_term
    scaled = gain * dnormed
    inner = jnp.mean(x_float * scaled, axis=-1, keepdims=True)
    result = (
        grad_in.astype(jnp.float32)
        + inverse * scaled
        - x_float * inverse * inverse * inverse * inner
    )
    return result.astype(jnp.bfloat16)


def shards(layer_inputs, top_grad, expert_ids, router, norm_gain, w_gate, w_up, w_down):
    segments = lax.axis_size("section")
    experts = lax.axis_size("expert")
    segment_index = lax.axis_index("section")
    micro = layer_inputs.shape[1]
    tok_rows = layer_inputs.shape[2]
    width = layer_inputs.shape[3]
    per_token = expert_ids.shape[3]
    capacity = min(tok_rows, per_token * tok_rows // experts + max(1, tok_rows // 16))
    slots = experts * capacity
    chunk = CHUNK if micro % CHUNK == 0 else 1
    chunks = micro // chunk
    lanes = 128
    gain = norm_gain[0].astype(jnp.float32)
    router_layer = router[0]
    gate_w = w_gate[0, 0]
    up_w = w_up[0, 0]
    down_w = w_down[0, 0]
    ids = expert_ids[0]
    x_float, inverse, normed = prepare(layer_inputs[0], gain)
    top_full = lax.all_gather(top_grad, "section", axis=0, tiled=True)

    select = jax.vmap(lambda i: selection(i, experts, capacity))(ids)
    sent_normed = pack_rows(select, normed, per_token).reshape(micro, experts, capacity, width)
    got_normed = exchange(sent_normed)
    rows = got_normed.reshape(micro * slots, width)
    gate = jnp.dot(rows, gate_w, preferred_element_type=jnp.float32)
    up_rows = jnp.dot(rows, up_w, preferred_element_type=jnp.float32)
    squash = jax.nn.sigmoid(gate)
    active = gate * squash
    hidden = (active * up_rows).astype(jnp.bfloat16)
    factor = up_rows * squash * (1.0 + gate * (1.0 - squash))
    hidden = hidden.reshape(micro, slots, -1)
    factor = factor.reshape(micro, slots, -1)
    active = active.reshape(micro, slots, -1)

    logits = jnp.dot(normed, router_layer, preferred_element_type=jnp.float32)
    raised = jnp.exp(logits)
    probs = raised / jnp.sum(raised, axis=-1, keepdims=True)
    choose = (ids[..., None] == jnp.arange(router_layer.shape[1], dtype=jnp.int32)).astype(
        jnp.float32
    )
    picked = jnp.sum(probs[..., None, :] * choose, axis=-1)

    def take(values, start):
        return lax.dynamic_slice_in_dim(values, start, chunk, 0)

    def advance(step, carry):
        previous, collected = carry
        arrived = shifted(previous, "section", -1)
        position = step - (segments - 1 - segment_index)
        working = jnp.logical_and(position >= 0, position < chunks)
        start = jnp.clip(position, 0, chunks - 1) * chunk
        grad_in = jnp.where(segment_index == segments - 1, take(top_full, start), arrived)
        select_now = take(select, start)
        sent_grad = pack_rows(select_now, grad_in, per_token).reshape(
            chunk, experts, capacity, width
        )
        got_grad = exchange(sent_grad)
        rows_grad = got_grad.reshape(chunk * slots, width)
        dhidden = lax.dot_general(
            rows_grad, down_w, (((1,), (1,)), ((), ())), preferred_element_type=jnp.float32
        )
        hidden_now = take(hidden, start).reshape(chunk * slots, -1)
        dprob = jnp.sum(hidden_now.astype(jnp.float32) * dhidden, axis=-1)
        factor_now = take(factor, start).reshape(chunk * slots, -1)
        active_now = take(active, start).reshape(chunk * slots, -1)
        dgate = (dhidden * factor_now).astype(jnp.bfloat16)
        dup = (dhidden * active_now).astype(jnp.bfloat16)
        returned = lax.dot_general(
            dgate, gate_w, (((1,), (1,)), ((), ())), preferred_element_type=jnp.float32
        )
        returned = returned + lax.dot_general(
            dup, up_w, (((1,), (1,)), ((), ())), preferred_element_type=jnp.float32
        )
        high = dprob.astype(jnp.bfloat16)
        low = (dprob - high.astype(jnp.float32)).astype(jnp.bfloat16)
        column = lax.broadcasted_iota(jnp.int32, (chunk * slots, lanes), 1)
        extra = jnp.where(column == 0, high[:, None], jnp.where(column == 1, low[:, None], 0))
        packed = jnp.concatenate([returned.astype(jnp.bfloat16), extra.astype(jnp.bfloat16)], axis=1)
        packed = packed.reshape(chunk, experts, capacity, width + lanes)
        back = exchange(packed)
        back = back.reshape(chunk, slots, width + lanes)
        pair = jnp.einsum("mps,msw->mpw", select_now, back, preferred_element_type=jnp.float32)
        pair_back = pair[..., :width].reshape(chunk, tok_rows, per_token, width)
        pair_prob = (pair[..., width] + pair[..., width + 1]).reshape(chunk, tok_rows, per_token)
        result = finish(
            take(x_float, start),
            take(inverse, start),
            gain,
            router_layer,
            take(probs, start),
            take(choose, start),
            take(picked, start),
            grad_in,
            pair_back,
            pair_prob,
        )
        retained = take(collected, start)
        collected = lax.dynamic_update_slice_in_dim(
            collected, jnp.where(working, result, retained), start, 0
        )
        return (result, collected)

    begin = (
        jnp.zeros((chunk, tok_rows, width), jnp.bfloat16),
        jnp.zeros((micro, tok_rows, width), jnp.bfloat16),
    )
    final_grad, collected = lax.fori_loop(0, chunks + segments - 1, advance, begin)
    return collected.reshape(1, micro, tok_rows, width)


def solution(mesh):
    placed = (
        P("section", None, "expert", None),
        P("section", "expert", None),
        P("section", None, "expert", None),
        P("section", None, None),
        P("section", None),
        P("section", "expert", None, None),
        P("section", "expert", None, None),
        P("section", "expert", None, None),
    )
    return jax.shard_map(
        shards,
        mesh=mesh,
        in_specs=placed,
        out_specs=P("section", None, "expert", None),
        check_vma=False,
    )
```

```python
import jax
import jax.numpy as jnp
from jax import lax
from jax.sharding import PartitionSpec as P

CHUNK = 2


def shifted(shard, axis, by):
    devices = lax.axis_size(axis)
    pairs = [(i, i + by) for i in range(devices) if 0 <= i + by < devices]
    return lax.ppermute(shard, axis, pairs)


def exchange(values):
    shape = values.shape
    folded = values.reshape(shape[:-1] + (shape[-1] // 128, 128))
    folded = lax.all_to_all(folded, "expert", split_axis=1, concat_axis=1, tiled=True)
    return folded.reshape(shape)


def prepare(x_rows, gain):
    x_float = x_rows.astype(jnp.float32)
    inverse = lax.rsqrt(jnp.mean(x_float * x_float, axis=-1, keepdims=True) + 1e-05)
    normed = (x_float * inverse * gain).astype(jnp.bfloat16)
    return (x_float, inverse, normed)


def selection(ids, experts, capacity):
    pair_ids = ids.reshape(-1)
    onehot = (pair_ids[:, None] == jnp.arange(experts, dtype=jnp.int32)[None, :]).astype(jnp.int32)
    ranks = jnp.sum(onehot * (jnp.cumsum(onehot, axis=0) - 1), axis=1)
    target = pair_ids * capacity + ranks
    return (target[:, None] == jnp.arange(experts * capacity, dtype=jnp.int32)[None, :]).astype(
        jnp.bfloat16
    )


def pack_rows(select, rows, per_token):
    repeated = jnp.repeat(rows, per_token, axis=1)
    packed = jnp.einsum("mps,mpw->msw", select, repeated, preferred_element_type=jnp.float32)
    return packed.astype(jnp.bfloat16)


def finish(x_float, inverse, gain, router_layer, probs, choose, picked, grad_in, pair_back, pair_prob):
    dfull = jnp.sum(pair_prob[..., None] * choose, axis=-2)
    dlogit = probs * (dfull - jnp.sum(probs * dfull, axis=-1, keepdims=True))
    router_term = jnp.dot(
        dlogit, router_layer.astype(jnp.float32).T, precision=lax.Precision.HIGHEST
    )
    dnormed = jnp.sum(picked[..., None] * pair_back, axis=-2) + router_term
    scaled = gain * dnormed
    inner = jnp.mean(x_float * scaled, axis=-1, keepdims=True)
    result = (
        grad_in.astype(jnp.float32)
        + inverse * scaled
        - x_float * inverse * inverse * inverse * inner
    )
    return result.astype(jnp.bfloat16)


def shards(layer_inputs, top_grad, expert_ids, router, norm_gain, w_gate, w_up, w_down):
    segments = lax.axis_size("section")
    experts = lax.axis_size("expert")
    segment_index = lax.axis_index("section")
    micro = layer_inputs.shape[1]
    tok_rows = layer_inputs.shape[2]
    width = layer_inputs.shape[3]
    per_token = expert_ids.shape[3]
    capacity = min(tok_rows, per_token * tok_rows // experts + max(1, tok_rows // 16))
    slots = experts * capacity
    chunk = CHUNK if micro % CHUNK == 0 else 1
    chunks = micro // chunk
    lanes = 128
    gain = norm_gain[0].astype(jnp.float32)
    router_layer = router[0]
    gate_w = w_gate[0, 0]
    up_w = w_up[0, 0]
    down_w = w_down[0, 0]
    ids = expert_ids[0]
    x_float, inverse, normed = prepare(layer_inputs[0], gain)
    top_full = lax.all_gather(top_grad, "section", axis=0, tiled=True)

    select = jax.vmap(lambda i: selection(i, experts, capacity))(ids)
    sent_normed = pack_rows(select, normed, per_token).reshape(micro, experts, capacity, width)
    got_normed = exchange(sent_normed)
    rows = got_normed.reshape(micro * slots, width)
    gate = jnp.dot(rows, gate_w, preferred_element_type=jnp.float32)
    up_rows = jnp.dot(rows, up_w, preferred_element_type=jnp.float32)
    squash = jax.nn.sigmoid(gate)
    active = gate * squash
    hidden = (active * up_rows).astype(jnp.bfloat16)
    factor = up_rows * squash * (1.0 + gate * (1.0 - squash))
    hidden = hidden.reshape(micro, slots, -1)
    factor = factor.reshape(micro, slots, -1)
    active = active.reshape(micro, slots, -1)

    logits = jnp.dot(normed, router_layer, preferred_element_type=jnp.float32)
    raised = jnp.exp(logits)
    probs = raised / jnp.sum(raised, axis=-1, keepdims=True)
    choose = (ids[..., None] == jnp.arange(router_layer.shape[1], dtype=jnp.int32)).astype(
        jnp.float32
    )
    picked = jnp.sum(probs[..., None, :] * choose, axis=-1)

    def take(values, start):
        return lax.dynamic_slice_in_dim(values, start, chunk, 0)

    def advance(step, carry):
        previous, collected = carry
        arrived = shifted(previous, "section", -1)
        position = step - (segments - 1 - segment_index)
        working = jnp.logical_and(position >= 0, position < chunks)
        start = jnp.clip(position, 0, chunks - 1) * chunk
        grad_in = jnp.where(segment_index == segments - 1, take(top_full, start), arrived)
        result = lax.cond(
            working,
            lambda operands: work(*operands),
            lambda operands: jnp.zeros_like(operands[1]),
            (start, grad_in),
        )
        retained = take(collected, start)
        collected = lax.dynamic_update_slice_in_dim(
            collected, jnp.where(working, result, retained), start, 0
        )
        return (result, collected)

    def work(start, grad_in):
        select_now = take(select, start)
        sent_grad = pack_rows(select_now, grad_in, per_token).reshape(
            chunk, experts, capacity, width
        )
        got_grad = exchange(sent_grad)
        rows_grad = got_grad.reshape(chunk * slots, width)
        dhidden = lax.dot_general(
            rows_grad, down_w, (((1,), (1,)), ((), ())), preferred_element_type=jnp.float32
        )
        hidden_now = take(hidden, start).reshape(chunk * slots, -1)
        dprob = jnp.sum(hidden_now.astype(jnp.float32) * dhidden, axis=-1)
        factor_now = take(factor, start).reshape(chunk * slots, -1)
        active_now = take(active, start).reshape(chunk * slots, -1)
        dgate = (dhidden * factor_now).astype(jnp.bfloat16)
        dup = (dhidden * active_now).astype(jnp.bfloat16)
        returned = lax.dot_general(
            dgate, gate_w, (((1,), (1,)), ((), ())), preferred_element_type=jnp.float32
        )
        returned = returned + lax.dot_general(
            dup, up_w, (((1,), (1,)), ((), ())), preferred_element_type=jnp.float32
        )
        high = dprob.astype(jnp.bfloat16)
        low = (dprob - high.astype(jnp.float32)).astype(jnp.bfloat16)
        column = lax.broadcasted_iota(jnp.int32, (chunk * slots, lanes), 1)
        extra = jnp.where(column == 0, high[:, None], jnp.where(column == 1, low[:, None], 0))
        packed = jnp.concatenate([returned.astype(jnp.bfloat16), extra.astype(jnp.bfloat16)], axis=1)
        packed = packed.reshape(chunk, experts, capacity, width + lanes)
        back = exchange(packed)
        back = back.reshape(chunk, slots, width + lanes)
        pair = jnp.einsum("mps,msw->mpw", select_now, back, preferred_element_type=jnp.float32)
        pair_back = pair[..., :width].reshape(chunk, tok_rows, per_token, width)
        pair_prob = (pair[..., width] + pair[..., width + 1]).reshape(chunk, tok_rows, per_token)
        result = finish(
            take(x_float, start),
            take(inverse, start),
            gain,
            router_layer,
            take(probs, start),
            take(choose, start),
            take(picked, start),
            grad_in,
            pair_back,
            pair_prob,
        )
        return result

    begin = (
        jnp.zeros((chunk, tok_rows, width), jnp.bfloat16),
        jnp.zeros((micro, tok_rows, width), jnp.bfloat16),
    )
    final_grad, collected = lax.fori_loop(0, chunks + segments - 1, advance, begin)
    return collected.reshape(1, micro, tok_rows, width)


def solution(mesh):
    placed = (
        P("section", None, "expert", None),
        P("section", "expert", None),
        P("section", None, "expert", None),
        P("section", None, None),
        P("section", None),
        P("section", "expert", None, None),
        P("section", "expert", None, None),
        P("section", "expert", None, None),
    )
    return jax.shard_map(
        shards,
        mesh=mesh,
        in_specs=placed,
        out_specs=P("section", None, "expert", None),
        check_vma=False,
    )
```
